512 devices in a mesh: seg: 64 (over y, z_lo, core), blk: 8 (over x, z_hi).
Axes of the slice: x: 4, y: 4, z: 16 (z_hi: 2, z_lo: 8; z = z_hi * 8 + z_lo), core: 2. Of those that a mesh axis runs over, the one named last changes fastest.
Arguments:
- record: float32 [24, 262144], P(None, ('seg', 'blk')), may hold values from -8 to 8, as said below
- templates: bfloat16 [128, 24, 512], P('blk'), may hold values from -6 to 6
Outputs:
- detection: float32 [128, 262144], P(None, ('seg', 'blk'))
The draws below stay inside these ranges and needn't reach their ends.
Inputs may be any that keep to these rules, and one draw needn't show every extreme that they name: `record`: network samples.
All inputs are finite; a program needn't handle non-finite values.
Results may differ from the reference program's by a relative error of at most 0.0032.
Values may be sent and summed in bfloat16 or wider, within the bound.
No kernel may reach another device: no remote copies, remote signals or barrier semaphores. Data moves between devices by JAX's collectives and lax.ppermute only.
A program may use at most 64 MiB of HBM per device.

```python
import math
import jax
import jax.numpy as jnp
from jax import lax

K = 128
C = 24
L = 512
NT = 262144


def template_shapes(key):
    base = jax.random.fold_in(key, 23)
    noise_key, tap_key, period_key, phase_key = jax.random.split(base, 4)
    raw = jnp.clip(jax.random.normal(noise_key, (K, C, L + 2), jnp.float32), -4.0, 4.0)
    taps = jax.random.uniform(tap_key, (2, K, 1, 1), jnp.float32, -0.8, 0.8)
    smooth = raw[:, :, :L] + taps[0] * raw[:, :, 1:L + 1] + taps[1] * raw[:, :, 2:L + 2]
    periods = jax.random.randint(period_key, (K, 1, 1), 10, 80).astype(jnp.int32)
    samples = jnp.arange(L, dtype=jnp.int32)[None, None, :]
    cycle = jnp.mod(samples, periods).astype(jnp.float32) / periods.astype(jnp.float32)
    phase = jax.random.uniform(phase_key, (K, C, 1), jnp.float32, -math.pi, math.pi)
    wave = jnp.sin(2.0 * math.pi * cycle + phase)
    return jnp.clip(smooth + wave, -6.0, 6.0)


def draw_templates(key, part):
    return template_shapes(key).astype(jnp.bfloat16)


def draw_record(key, part):
    shapes = template_shapes(key)
    base = jax.random.fold_in(key, 11)
    noise_key, tap_key, loud_key, period_key, phase_key, place_key, amp_key = jax.random.split(base, 7)
    dropout_key = jax.random.fold_in(key, 37)
    blocks = (NT + L - 1) // L
    positions = jnp.arange(NT, dtype=jnp.int32)
    moments = positions.astype(jnp.float32)
    block_of = positions // L
    noise = jnp.clip(jax.random.normal(noise_key, (C, NT + 2), jnp.float32), -4.0, 4.0)
    rising = 0.25 + 1.5 * moments / NT
    taps = jax.random.uniform(tap_key, (2, C, blocks), jnp.float32, -0.8, 0.8)
    first_tap = taps[0][:, block_of]
    second_tap = taps[1][:, block_of]
    colored = noise[:, :NT] + first_tap * noise[:, 1:NT + 1] + second_tap * noise[:, 2:NT + 2]
    loudness = jnp.exp(jax.random.uniform(loud_key, (C, blocks), jnp.float32, math.log(0.5), math.log(1.6)))
    colored = colored * loudness[:, block_of]
    periods = jax.random.randint(period_key, (C, 1), 12, 90).astype(jnp.int32)
    cycle = jnp.mod(positions[None, :], periods).astype(jnp.float32) / periods.astype(jnp.float32)
    phase = jax.random.uniform(phase_key, (C, 1), jnp.float32, -math.pi, math.pi)
    tone = 0.6 * jnp.sin(2.0 * math.pi * cycle + phase)
    values = colored + rising[None, :] * tone
    starts = jax.random.randint(place_key, (K,), 0, NT - L + 1).astype(jnp.int32)
    amplitudes = jax.random.uniform(amp_key, (K,), jnp.float32, 0.4, 1.2)

    def add_event(index, track):
        begin = starts[index]
        zero_index = jnp.zeros((), jnp.int32)
        old = lax.dynamic_slice(track, (zero_index, begin), (C, L))
        return lax.dynamic_update_slice(track, old + amplitudes[index] * shapes[index], (zero_index, begin))
    track = lax.fori_loop(0, K, add_event, jnp.zeros((C, NT), jnp.float32))
    values = values + track
    dropout_len = 4 * L
    drop_starts = jax.random.randint(dropout_key, (C, 1), 0, NT - dropout_len)
    inside = jnp.logical_and(positions[None, :] >= drop_starts, positions[None, :] < drop_starts + dropout_len)
    values = jnp.where(inside, jnp.zeros_like(values), values)
    return jnp.clip(values, -8.0, 8.0)


def setup_inputs(seed: int = 0) -> dict:
    key_of = jax.random.split(jax.random.key(seed), 3)
    return {
        "record": draw_record(jax.random.fold_in(key_of[2], 71), 0),
        "templates": draw_templates(jax.random.fold_in(key_of[2], 71), 0),
    }


def normalize(templates):
    widened = templates.astype(jnp.float32)
    centred = widened - lax.optimization_barrier(jnp.mean(widened, axis=2, keepdims=True))
    return (centred / jnp.sqrt(lax.optimization_barrier(jnp.sum(centred * centred, axis=2, keepdims=True)) + 1e-06)).astype(jnp.bfloat16)

def window_scale(extended, window):
    zero = jnp.zeros((), extended.dtype)
    window_sum = lax.reduce_window(extended, zero, lax.add, (1, window), (1, 1), 'VALID')
    window_sq = lax.reduce_window(extended * extended, zero, lax.add, (1, window), (1, 1), 'VALID')
    spread = window_sq - window_sum * window_sum / window
    return 1.0 / jnp.sqrt(jnp.maximum(spread, 1.0))

def reference(record, templates):
    normalized = normalize(templates)
    padded_rec = jnp.pad(record, ((0, 0), (0, L - 1)))
    scale = window_scale(padded_rec, L)
    record_bf = lax.optimization_barrier(record.astype(jnp.bfloat16))
    widened = record_bf.astype(jnp.float32)
    fft_size = 1 << (NT + L).bit_length()
    spectrum = jnp.fft.rfft(widened, n=fft_size, axis=1)

    def score_one(kernel):
        kernel_spec = jnp.fft.rfft(kernel.astype(jnp.float32), n=fft_size, axis=1)
        raw_corr = jnp.fft.irfft(jnp.conj(kernel_spec) * spectrum, n=fft_size, axis=1)[:, :NT]
        return lax.optimization_barrier(jnp.sum(raw_corr * scale, axis=0)) / C
    stacked = lax.map(score_one, normalized)
    power_sum = lax.optimization_barrier(jnp.sum(stacked * stacked, axis=1))
    return stacked / jnp.sqrt(power_sum / NT + 1e-06)[:, None]
```

```python
import jax
import jax.numpy as jnp
from jax import lax
from jax.experimental import pallas as pl
from jax.experimental.pallas import tpu as pltpu
from jax.sharding import PartitionSpec as P

LAG_BLOCK = 128


def normalize(templates):
    widened = templates.astype(jnp.float32)
    centred = widened - jnp.mean(widened, axis=2, keepdims=True)
    return (centred / jnp.sqrt(jnp.sum(centred * centred, axis=2, keepdims=True) + 1e-06)).astype(
        jnp.bfloat16
    )


def gather_group(record, axis):
    size = lax.axis_size(axis)
    pieces = [record]
    for d in range(1, size):
        pieces.append(lax.ppermute(record, axis, [(i, (i + d) % size) for i in range(size)]))
    slots = jnp.stack(pieces)
    me = lax.axis_index(axis)
    order = (me - jnp.arange(size)) % size
    group = jnp.take(slots, order, axis=0)
    channels, samples = record.shape
    return jnp.transpose(group, (1, 0, 2)).reshape(channels, size * samples)


def next_group_head(record):
    nseg = lax.axis_size("seg")
    nblk = lax.axis_size("blk")
    total = jnp.zeros_like(record)
    for dest in range(nblk):
        route = [((s + 1) * nblk, s * nblk + dest) for s in range(nseg - 1)]
        total = total + lax.ppermute(record, ("seg", "blk"), route)
    return total


def window_scale(extended, window, outputs):
    channels = extended.shape[0]
    blocks = outputs // window
    rows = jnp.arange(2 * window, dtype=jnp.int32)[:, None]
    cols = jnp.arange(window, dtype=jnp.int32)[None, :]
    band = jnp.logical_and(rows >= cols, rows < cols + window).astype(jnp.float32)
    both = jnp.concatenate([extended, extended * extended], axis=0)
    pairs = jnp.stack([both[:, m * window : (m + 2) * window] for m in range(blocks)], axis=1)
    sums = jnp.dot(
        pairs.reshape(2 * channels * blocks, 2 * window),
        band,
        precision=lax.Precision.HIGHEST,
        preferred_element_type=jnp.float32,
    ).reshape(2 * channels, outputs)
    window_sum = sums[:channels]
    window_sq = sums[channels:]
    spread = window_sq - window_sum * window_sum / window
    return 1.0 / jnp.sqrt(jnp.maximum(spread, 1.0))


def corr_kernel(rec_ref, tr_ref, scale_ref, out_ref):
    channels, _, width = rec_ref.shape
    lag = tr_ref.shape[2]
    members, samples = out_ref.shape
    parts = tr_ref.shape[1] // members
    span = samples + (parts - 1) * lag

    def one_channel(c, acc):
        row = rec_ref[c]
        wide = jnp.broadcast_to(row, (lag, width))
        hankel = pltpu.roll(wide, width - (lag - 1), 1, stride=1, stride_axis=0)
        hankel = hankel[:, :span].astype(jnp.bfloat16)
        prod = jnp.dot(tr_ref[c], hankel, preferred_element_type=jnp.float32)
        raw = prod[0:members, 0:samples]
        for a in range(1, parts):
            raw = raw + prod[a * members : (a + 1) * members, a * lag : a * lag + samples]
        return acc + raw * scale_ref[c]

    acc = lax.fori_loop(0, channels, one_channel, jnp.zeros((members, samples), jnp.float32))
    out_ref[...] = acc / channels


def stacked_correlation(rec_bf, normalized, scale):
    members, channels, window = normalized.shape
    parts = window // LAG_BLOCK
    kernels = normalized.reshape(members, channels, parts, LAG_BLOCK)[..., ::-1]
    kernels = jnp.transpose(kernels, (1, 2, 0, 3)).reshape(channels, parts * members, LAG_BLOCK)
    samples = scale.shape[1]
    return pl.pallas_call(
        corr_kernel,
        out_shape=jax.ShapeDtypeStruct((members, samples), jnp.float32),
    )(rec_bf[:, None, :], kernels, scale[:, None, :])


def seg_sum(value):
    nseg = lax.axis_size("seg")
    if nseg & (nseg - 1):
        return lax.psum(value, "seg")
    bit = 1
    while bit < nseg:
        value = value + lax.ppermute(value, "seg", [(i, i ^ bit) for i in range(nseg)])
        bit *= 2
    return value


def body(record, templates):
    channels, samples = record.shape
    window = templates.shape[2]
    nblk = lax.axis_size("blk")
    group = gather_group(record, "blk")
    head = next_group_head(record)
    extended = jnp.concatenate([group, head], axis=1)
    outputs = group.shape[1]
    scale = window_scale(extended, window, outputs)
    rec_bf = extended.astype(jnp.bfloat16).astype(jnp.float32)
    normalized = normalize(templates)
    stacked = stacked_correlation(rec_bf, normalized, scale)
    power_sum = seg_sum(jnp.sum(stacked * stacked, axis=1))
    record_len = samples * lax.axis_size("seg") * nblk
    detection = stacked / jnp.sqrt(power_sum / record_len + 1e-06)[:, None]
    members = detection.shape[0]
    pieces = detection.reshape(members, nblk, samples)
    spread = lax.all_to_all(pieces, "blk", 1, 0, tiled=True)
    return spread.reshape(members * nblk, samples)


def solution(mesh):
    return jax.shard_map(
        body,
        mesh=mesh,
        in_specs=(P(None, ("seg", "blk")), P("blk", None, None)),
        out_specs=P(None, ("seg", "blk")),
        check_vma=False,
    )
```

```python
import jax
import jax.numpy as jnp
from jax import lax
from jax.experimental import pallas as pl
from jax.experimental.pallas import tpu as pltpu
from jax.sharding import PartitionSpec as P

LAG_BLOCK = 128


def normalize(templates):
    widened = templates.astype(jnp.float32)
    centred = widened - jnp.mean(widened, axis=2, keepdims=True)
    return (centred / jnp.sqrt(jnp.sum(centred * centred, axis=2, keepdims=True) + 1e-06)).astype(
        jnp.bfloat16
    )


def gather_group(record, axis):
    size = lax.axis_size(axis)
    channels, samples = record.shape
    copies = jnp.broadcast_to(record[None], (size, channels, samples))
    group = lax.all_to_all(copies, axis, 0, 0, tiled=True)
    return jnp.transpose(group, (1, 0, 2)).reshape(channels, size * samples)


def next_group_head(record):
    nseg = lax.axis_size("seg")
    nblk = lax.axis_size("blk")
    total = jnp.zeros_like(record)
    for dest in range(nblk):
        route = [((s + 1) * nblk, s * nblk + dest) for s in range(nseg - 1)]
        total = total + lax.ppermute(record, ("seg", "blk"), route)
    return total


def window_scale(extended, window, outputs):
    channels = extended.shape[0]
    blocks = outputs // window
    rows = jnp.arange(2 * window, dtype=jnp.int32)[:, None]
    cols = jnp.arange(window, dtype=jnp.int32)[None, :]
    band = jnp.logical_and(rows >= cols, rows < cols + window).astype(jnp.float32)
    both = jnp.concatenate([extended, extended * extended], axis=0)
    pairs = jnp.stack([both[:, m * window : (m + 2) * window] for m in range(blocks)], axis=1)
    sums = jnp.dot(
        pairs.reshape(2 * channels * blocks, 2 * window),
        band,
        precision=lax.Precision.HIGHEST,
        preferred_element_type=jnp.float32,
    ).reshape(2 * channels, outputs)
    window_sum = sums[:channels]
    window_sq = sums[channels:]
    spread = window_sq - window_sum * window_sum / window
    return 1.0 / jnp.sqrt(jnp.maximum(spread, 1.0))


def corr_kernel(rec_ref, tr_ref, scale_ref, out_ref):
    channels, _, width = rec_ref.shape
    lag = tr_ref.shape[2]
    members, samples = out_ref.shape
    parts = tr_ref.shape[1] // members
    span = samples + (parts - 1) * lag

    def one_channel(c, acc):
        row = rec_ref[c]
        wide = jnp.broadcast_to(row, (lag, width))
        hankel = pltpu.roll(wide, width - (lag - 1), 1, stride=1, stride_axis=0)
        hankel = hankel[:, :span].astype(jnp.bfloat16)
        prod = jnp.dot(tr_ref[c], hankel, preferred_element_type=jnp.float32)
        raw = prod[0:members, 0:samples]
        for a in range(1, parts):
            raw = raw + prod[a * members : (a + 1) * members, a * lag : a * lag + samples]
        return acc + raw * scale_ref[c]

    acc = lax.fori_loop(0, channels, one_channel, jnp.zeros((members, samples), jnp.float32))
    out_ref[...] = acc / channels


def stacked_correlation(rec_bf, normalized, scale):
    members, channels, window = normalized.shape
    parts = window // LAG_BLOCK
    kernels = normalized.reshape(members, channels, parts, LAG_BLOCK)[..., ::-1]
    kernels = jnp.transpose(kernels, (1, 2, 0, 3)).reshape(channels, parts * members, LAG_BLOCK)
    samples = scale.shape[1]
    return pl.pallas_call(
        corr_kernel,
        out_shape=jax.ShapeDtypeStruct((members, samples), jnp.float32),
    )(rec_bf[:, None, :], kernels, scale[:, None, :])


def seg_sum(value):
    nseg = lax.axis_size("seg")
    copies = jnp.broadcast_to(value[None], (nseg,) + value.shape)
    return jnp.sum(lax.all_to_all(copies, "seg", 0, 0, tiled=True), axis=0)


def body(record, templates):
    channels, samples = record.shape
    window = templates.shape[2]
    nblk = lax.axis_size("blk")
    head = next_group_head(record)
    group = gather_group(record, "blk")
    extended = jnp.concatenate([group, head], axis=1)
    outputs = group.shape[1]
    scale = window_scale(extended, window, outputs)
    rec_bf = extended.astype(jnp.bfloat16).astype(jnp.float32)
    normalized = normalize(templates)
    stacked = stacked_correlation(rec_bf, normalized, scale)
    power_sum = seg_sum(jnp.sum(stacked * stacked, axis=1))
    record_len = samples * lax.axis_size("seg") * nblk
    detection = stacked / jnp.sqrt(power_sum / record_len + 1e-06)[:, None]
    members = detection.shape[0]
    pieces = detection.reshape(members, nblk, samples)
    spread = lax.all_to_all(pieces, "blk", 1, 0, tiled=True)
    return spread.reshape(members * nblk, samples)


def solution(mesh):
    return jax.shard_map(
        body,
        mesh=mesh,
        in_specs=(P(None, ("seg", "blk")), P("blk", None, None)),
        out_specs=P(None, ("seg", "blk")),
        check_vma=False,
    )
```

```python
import jax
import jax.numpy as jnp
from jax import lax
from jax.experimental import pallas as pl
from jax.experimental.pallas import tpu as pltpu
from jax.sharding import PartitionSpec as P

LAG_BLOCK = 128


def normalize(templates):
    widened = templates.astype(jnp.float32)
    centred = widened - jnp.mean(widened, axis=2, keepdims=True)
    return (centred / jnp.sqrt(jnp.sum(centred * centred, axis=2, keepdims=True) + 1e-06)).astype(
        jnp.bfloat16
    )


def gather_group(record, axis):
    size = lax.axis_size(axis)
    channels, samples = record.shape
    copies = jnp.broadcast_to(record[None], (size, channels, samples))
    group = lax.all_to_all(copies, axis, 0, 0, tiled=True)
    return jnp.transpose(group, (1, 0, 2)).reshape(channels, size * samples)


def next_group_head(group, samples):
    nseg = lax.axis_size("seg")
    return lax.ppermute(group[:, :samples], "seg", [(i + 1, i) for i in range(nseg - 1)])


def window_scale(extended, window, outputs):
    channels = extended.shape[0]
    blocks = outputs // window
    rows = jnp.arange(2 * window, dtype=jnp.int32)[:, None]
    cols = jnp.arange(window, dtype=jnp.int32)[None, :]
    band = jnp.logical_and(rows >= cols, rows < cols + window).astype(jnp.float32)
    both = jnp.concatenate([extended, extended * extended], axis=0)
    pairs = jnp.stack([both[:, m * window : (m + 2) * window] for m in range(blocks)], axis=1)
    sums = jnp.dot(
        pairs.reshape(2 * channels * blocks, 2 * window),
        band,
        precision=lax.Precision.HIGHEST,
        preferred_element_type=jnp.float32,
    ).reshape(2 * channels, outputs)
    window_sum = sums[:channels]
    window_sq = sums[channels:]
    spread = window_sq - window_sum * window_sum / window
    return 1.0 / jnp.sqrt(jnp.maximum(spread, 1.0))


ROWS = 8


def corr_kernel(rec_ref, tr_ref, scale_ref, out_ref):
    channels, width = rec_ref.shape
    lag = tr_ref.shape[2]
    members, samples = out_ref.shape
    parts = tr_ref.shape[1] // members
    span = samples + (parts - 1) * lag

    def one_group(g, acc):
        first = pl.multiple_of(g * ROWS, ROWS)
        rows = rec_ref[pl.ds(first, ROWS), :]
        factors = scale_ref[pl.ds(first, ROWS), :]
        for r in range(ROWS):
            wide = jnp.broadcast_to(rows[r : r + 1, :], (lag, width))
            hankel = pltpu.roll(wide, width - (lag - 1), 1, stride=1, stride_axis=0)
            hankel = hankel[:, :span].astype(jnp.bfloat16)
            prod = jnp.dot(tr_ref[first + r], hankel, preferred_element_type=jnp.float32)
            raw = prod[0:members, 0:samples]
            for a in range(1, parts):
                raw = raw + prod[a * members : (a + 1) * members, a * lag : a * lag + samples]
            acc = acc + raw * factors[r : r + 1, :]
        return acc

    acc = lax.fori_loop(0, channels // ROWS, one_group, jnp.zeros((members, samples), jnp.float32))
    out_ref[...] = acc / channels


def lag_kernels(normalized):
    members, channels, window = normalized.shape
    parts = window // LAG_BLOCK
    kernels = normalized.reshape(members, channels, parts, LAG_BLOCK)[..., ::-1]
    return jnp.transpose(kernels, (1, 2, 0, 3)).reshape(channels, parts * members, LAG_BLOCK)


def stacked_correlation(extended, kernels, window, outputs):
    members = kernels.shape[1] * LAG_BLOCK // window
    scale = window_scale(extended, window, outputs)
    rec_bf = extended.astype(jnp.bfloat16).astype(jnp.float32)
    return pl.pallas_call(
        corr_kernel,
        out_shape=jax.ShapeDtypeStruct((members, outputs), jnp.float32),
    )(rec_bf, kernels, scale)


def seg_sum(value):
    nseg = lax.axis_size("seg")
    copies = jnp.broadcast_to(value[None], (nseg,) + value.shape)
    return jnp.sum(lax.all_to_all(copies, "seg", 0, 0, tiled=True), axis=0)


def body(record, templates):
    channels, samples = record.shape
    window = templates.shape[2]
    nblk = lax.axis_size("blk")
    group = gather_group(record, "blk")
    head = next_group_head(group, samples)
    kernels = lag_kernels(normalize(templates))
    inner = group.shape[1] - samples
    early = stacked_correlation(group, kernels, window, inner)
    tail = jnp.concatenate([group[:, inner:], head], axis=1)
    late = stacked_correlation(tail, kernels, window, samples)
    stacked = jnp.concatenate([early, late], axis=1)
    power_sum = seg_sum(jnp.sum(stacked * stacked, axis=1))
    record_len = samples * lax.axis_size("seg") * nblk
    detection = stacked / jnp.sqrt(power_sum / record_len + 1e-06)[:, None]
    members = detection.shape[0]
    pieces = detection.reshape(members, nblk, samples)
    spread = lax.all_to_all(pieces, "blk", 1, 0, tiled=True)
    return spread.reshape(members * nblk, samples)


def solution(mesh):
    return jax.shard_map(
        body,
        mesh=mesh,
        in_specs=(P(None, ("seg", "blk")), P("blk", None, None)),
        out_specs=P(None, ("seg", "blk")),
        check_vma=False,
    )
```

```python
import jax
import jax.numpy as jnp
from jax import lax
from jax.experimental import pallas as pl
from jax.experimental.pallas import tpu as pltpu
from jax.sharding import PartitionSpec as P

LAG_BLOCK = 64


def normalize(templates):
    widened = templates.astype(jnp.float32)
    centred = widened - jnp.mean(widened, axis=2, keepdims=True)
    return (centred / jnp.sqrt(jnp.sum(centred * centred, axis=2, keepdims=True) + 1e-06)).astype(
        jnp.bfloat16
    )


def gather_group(record, axis):
    size = lax.axis_size(axis)
    channels, samples = record.shape
    copies = jnp.broadcast_to(record[None], (size, channels, samples))
    group = lax.all_to_all(copies, axis, 0, 0, tiled=True)
    return jnp.transpose(group, (1, 0, 2)).reshape(channels, size * samples)


def next_group_head(group, samples):
    nseg = lax.axis_size("seg")
    return lax.ppermute(group[:, :samples], "seg", [(i + 1, i) for i in range(nseg - 1)])


def window_scale(extended, window, outputs):
    channels = extended.shape[0]
    blocks = outputs // window
    rows = jnp.arange(2 * window, dtype=jnp.int32)[:, None]
    cols = jnp.arange(window, dtype=jnp.int32)[None, :]
    band = jnp.logical_and(rows >= cols, rows < cols + window).astype(jnp.float32)
    both = jnp.concatenate([extended, extended * extended], axis=0)
    pairs = jnp.stack([both[:, m * window : (m + 2) * window] for m in range(blocks)], axis=1)
    sums = jnp.dot(
        pairs.reshape(2 * channels * blocks, 2 * window),
        band,
        precision=lax.Precision.HIGHEST,
        preferred_element_type=jnp.float32,
    ).reshape(2 * channels, outputs)
    window_sum = sums[:channels]
    window_sq = sums[channels:]
    spread = window_sq - window_sum * window_sum / window
    return 1.0 / jnp.sqrt(jnp.maximum(spread, 1.0))


ROWS = 8


def corr_kernel(rec_ref, tr_ref, even_scale_ref, odd_scale_ref, out_ref):
    channels, width = rec_ref.shape
    lag = tr_ref.shape[2]
    members, samples = out_ref.shape
    parts = tr_ref.shape[1] // members
    span = samples + parts * lag
    odd_width = samples + 2 * lag

    def one_group(g, carry):
        even_acc, odd_acc = carry
        first = pl.multiple_of(g * ROWS, ROWS)
        rows = rec_ref[pl.ds(first, ROWS), :]
        even_factors = even_scale_ref[pl.ds(first, ROWS), :]
        odd_factors = odd_scale_ref[pl.ds(first, ROWS), :]
        for r in range(ROWS):
            wide = jnp.broadcast_to(rows[r : r + 1, :], (lag, width))
            hankel = pltpu.roll(wide, width - (lag - 1), 1, stride=1, stride_axis=0)
            hankel = hankel[:, :span].astype(jnp.bfloat16)
            prod = jnp.dot(tr_ref[first + r], hankel, preferred_element_type=jnp.float32)
            even = prod[0:members, 0:samples]
            odd = prod[members : 2 * members, 0:odd_width]
            for i in range(1, parts // 2):
                lo = 2 * i * members
                even = even + prod[lo : lo + members, 2 * i * lag : 2 * i * lag + samples]
                odd = odd + prod[lo + members : lo + 2 * members, 2 * i * lag : 2 * i * lag + odd_width]
            even_acc = even_acc + even * even_factors[r : r + 1, :]
            odd_acc = odd_acc + odd * odd_factors[r : r + 1, :]
        return even_acc, odd_acc

    start = (
        jnp.zeros((members, samples), jnp.float32),
        jnp.zeros((members, odd_width), jnp.float32),
    )
    even_acc, odd_acc = lax.fori_loop(0, channels // ROWS, one_group, start)
    out_ref[...] = (even_acc + odd_acc[:, lag : lag + samples]) / channels


def lag_kernels(normalized):
    members, channels, window = normalized.shape
    parts = window // LAG_BLOCK
    kernels = normalized.reshape(members, channels, parts, LAG_BLOCK)[..., ::-1]
    return jnp.transpose(kernels, (1, 2, 0, 3)).reshape(channels, parts * members, LAG_BLOCK)


def stacked_correlation(extended, kernels, window, outputs):
    members = kernels.shape[1] * LAG_BLOCK // window
    scale = window_scale(extended, window, outputs)
    odd_scale = jnp.pad(scale, ((0, 0), (LAG_BLOCK, LAG_BLOCK)))
    width = outputs + window + 2 * LAG_BLOCK
    padded = jnp.pad(extended, ((0, 0), (0, width - extended.shape[1])))
    rec_bf = padded.astype(jnp.bfloat16).astype(jnp.float32)
    return pl.pallas_call(
        corr_kernel,
        out_shape=jax.ShapeDtypeStruct((members, outputs), jnp.float32),
    )(rec_bf, kernels, scale, odd_scale)


def seg_sum(value):
    nseg = lax.axis_size("seg")
    copies = jnp.broadcast_to(value[None], (nseg,) + value.shape)
    return jnp.sum(lax.all_to_all(copies, "seg", 0, 0, tiled=True), axis=0)


def body(record, templates):
    channels, samples = record.shape
    window = templates.shape[2]
    nblk = lax.axis_size("blk")
    group = gather_group(record, "blk")
    head = next_group_head(group, samples)
    kernels = lag_kernels(normalize(templates))
    inner = group.shape[1] - samples
    early = stacked_correlation(group, kernels, window, inner)
    tail = jnp.concatenate([group[:, inner:], head], axis=1)
    late = stacked_correlation(tail, kernels, window, samples)
    stacked = jnp.concatenate([early, late], axis=1)
    power_sum = seg_sum(jnp.sum(stacked * stacked, axis=1))
    record_len = samples * lax.axis_size("seg") * nblk
    detection = stacked / jnp.sqrt(power_sum / record_len + 1e-06)[:, None]
    members = detection.shape[0]
    pieces = detection.astype(jnp.bfloat16).reshape(members, nblk, samples)
    spread = lax.all_to_all(pieces, "blk", 1, 0, tiled=True)
    return spread.reshape(members * nblk, samples).astype(jnp.float32)


def solution(mesh):
    return jax.shard_map(
        body,
        mesh=mesh,
        in_specs=(P(None, ("seg", "blk")), P("blk", None, None)),
        out_specs=P(None, ("seg", "blk")),
        check_vma=False,
    )
```

```python
import jax
import jax.numpy as jnp
from jax import lax
from jax.experimental import pallas as pl
from jax.experimental.pallas import tpu as pltpu
from jax.sharding import PartitionSpec as P

LAG_BLOCK = 64


def normalize(templates):
    widened = templates.astype(jnp.float32)
    centred = widened - jnp.mean(widened, axis=2, keepdims=True)
    return (centred / jnp.sqrt(jnp.sum(centred * centred, axis=2, keepdims=True) + 1e-06)).astype(
        jnp.bfloat16
    )


def gather_group(record, axis):
    size = lax.axis_size(axis)
    channels, samples = record.shape
    copies = jnp.broadcast_to(record[None], (size, channels, samples))
    group = lax.all_to_all(copies, axis, 0, 0, tiled=True)
    return jnp.transpose(group, (1, 0, 2)).reshape(channels, size * samples)


def next_group_head(group, samples):
    nseg = lax.axis_size("seg")
    return lax.ppermute(group[:, :samples], "seg", [(i + 1, i) for i in range(nseg - 1)])


def window_scale(extended, window, outputs):
    channels = extended.shape[0]
    blocks = outputs // window
    rows = jnp.arange(2 * window, dtype=jnp.int32)[:, None]
    cols = jnp.arange(window, dtype=jnp.int32)[None, :]
    band = jnp.logical_and(rows >= cols, rows < cols + window).astype(jnp.float32)
    both = jnp.concatenate([extended, extended * extended], axis=0)
    pairs = jnp.stack([both[:, m * window : (m + 2) * window] for m in range(blocks)], axis=1)
    sums = jnp.dot(
        pairs.reshape(2 * channels * blocks, 2 * window),
        band,
        precision=lax.Precision.HIGHEST,
        preferred_element_type=jnp.float32,
    ).reshape(2 * channels, outputs)
    window_sum = sums[:channels]
    window_sq = sums[channels:]
    spread = window_sq - window_sum * window_sum / window
    return 1.0 / jnp.sqrt(jnp.maximum(spread, 1.0))


ROWS = 8


def corr_kernel(rec_ref, tr_ref, scale_ref, out_ref):
    channels, width = rec_ref.shape
    lag = tr_ref.shape[2]
    members, samples = out_ref.shape
    parts = tr_ref.shape[1] // members
    span = samples + parts * lag
    odd_width = samples + 2 * lag

    def one_group(g, carry):
        even_acc, odd_acc = carry
        first = pl.multiple_of(g * ROWS, ROWS)
        rows = rec_ref[pl.ds(first, ROWS), :]
        even_factors = scale_ref[pl.ds(first, ROWS), :]
        blank = jnp.zeros((ROWS, 2 * lag), jnp.float32)
        odd_factors = pltpu.roll(jnp.concatenate([even_factors, blank], axis=1), lag, 1)
        for r in range(ROWS):
            wide = jnp.broadcast_to(rows[r : r + 1, :], (lag, width))
            hankel = pltpu.roll(wide, width - (lag - 1), 1, stride=1, stride_axis=0)
            hankel = hankel[:, :span].astype(jnp.bfloat16)
            prod = jnp.dot(tr_ref[first + r], hankel, preferred_element_type=jnp.float32)
            even = prod[0:members, 0:samples]
            odd = prod[members : 2 * members, 0:odd_width]
            for i in range(1, parts // 2):
                lo = 2 * i * members
                even = even + prod[lo : lo + members, 2 * i * lag : 2 * i * lag + samples]
                odd = odd + prod[lo + members : lo + 2 * members, 2 * i * lag : 2 * i * lag + odd_width]
            even_acc = even_acc + even * even_factors[r : r + 1, :]
            odd_acc = odd_acc + odd * odd_factors[r : r + 1, :]
        return even_acc, odd_acc

    start = (
        jnp.zeros((members, samples), jnp.float32),
        jnp.zeros((members, odd_width), jnp.float32),
    )
    even_acc, odd_acc = lax.fori_loop(0, channels // ROWS, one_group, start)
    out_ref[...] = (even_acc + odd_acc[:, lag : lag + samples]) / channels


def lag_kernels(normalized):
    members, channels, window = normalized.shape
    parts = window // LAG_BLOCK
    kernels = normalized.reshape(members, channels, parts, LAG_BLOCK)[..., ::-1]
    return jnp.transpose(kernels, (1, 2, 0, 3)).reshape(channels, parts * members, LAG_BLOCK)


def stacked_correlation(extended, kernels, window, outputs):
    members = kernels.shape[1] * LAG_BLOCK // window
    scale = window_scale(extended, window, outputs)
    return pl.pallas_call(
        corr_kernel,
        out_shape=jax.ShapeDtypeStruct((members, outputs), jnp.float32),
    )(extended, kernels, scale)


def seg_sum(value):
    nseg = lax.axis_size("seg")
    copies = jnp.broadcast_to(value[None], (nseg,) + value.shape)
    return jnp.sum(lax.all_to_all(copies, "seg", 0, 0, tiled=True), axis=0)


def body(record, templates):
    channels, samples = record.shape
    window = templates.shape[2]
    nblk = lax.axis_size("blk")
    group = gather_group(record, "blk")
    head = next_group_head(group, samples)
    kernels = lag_kernels(normalize(templates))
    inner = group.shape[1] - samples
    early = stacked_correlation(group, kernels, window, inner)
    tail = jnp.concatenate([group[:, inner:], head], axis=1)
    late = stacked_correlation(tail, kernels, window, samples)
    stacked = jnp.concatenate([early, late], axis=1)
    power_sum = seg_sum(jnp.sum(stacked * stacked, axis=1))
    record_len = samples * lax.axis_size("seg") * nblk
    detection = stacked / jnp.sqrt(power_sum / record_len + 1e-06)[:, None]
    members = detection.shape[0]
    pieces = detection.reshape(members, nblk, samples)
    spread = lax.all_to_all(pieces, "blk", 1, 0, tiled=True)
    return spread.reshape(members * nblk, samples)


def solution(mesh):
    return jax.shard_map(
        body,
        mesh=mesh,
        in_specs=(P(None, ("seg", "blk")), P("blk", None, None)),
        out_specs=P(None, ("seg", "blk")),
        check_vma=False,
    )
```

```python
import jax
import jax.numpy as jnp
from jax import lax
from jax.experimental import pallas as pl
from jax.experimental.pallas import tpu as pltpu
import numpy as np
from jax.sharding import Mesh, PartitionSpec as P

LAG_BLOCK = 64


def normalize(templates):
    widened = templates.astype(jnp.float32)
    centred = widened - jnp.mean(widened, axis=2, keepdims=True)
    return (centred / jnp.sqrt(jnp.sum(centred * centred, axis=2, keepdims=True) + 1e-06)).astype(
        jnp.bfloat16
    )


def gather_group(record):
    partner = lax.ppermute(record, "bz", [(0, 1), (1, 0)])
    low = lax.axis_index("bz") == 0
    pair = jnp.where(low, jnp.concatenate([record, partner], axis=1), jnp.concatenate([partner, record], axis=1))
    size = lax.axis_size("bx")
    channels, width = pair.shape
    copies = jnp.broadcast_to(pair[None], (size, channels, width))
    group = lax.all_to_all(copies, "bx", 0, 0, tiled=True)
    return jnp.transpose(group, (1, 0, 2)).reshape(channels, size * width)


def next_group_head(group, samples):
    nseg = lax.axis_size("seg")
    return lax.ppermute(group[:, :samples], "seg", [(i + 1, i) for i in range(nseg - 1)])


def window_scale(extended, window, outputs):
    channels = extended.shape[0]
    blocks = outputs // window
    rows = jnp.arange(2 * window, dtype=jnp.int32)[:, None]
    cols = jnp.arange(window, dtype=jnp.int32)[None, :]
    band = jnp.logical_and(rows >= cols, rows < cols + window).astype(jnp.float32)
    both = jnp.concatenate([extended, extended * extended], axis=0)
    pairs = jnp.stack([both[:, m * window : (m + 2) * window] for m in range(blocks)], axis=1)
    sums = jnp.dot(
        pairs.reshape(2 * channels * blocks, 2 * window),
        band,
        precision=lax.Precision.HIGHEST,
        preferred_element_type=jnp.float32,
    ).reshape(2 * channels, outputs)
    window_sum = sums[:channels]
    window_sq = sums[channels:]
    spread = window_sq - window_sum * window_sum / window
    return 1.0 / jnp.sqrt(jnp.maximum(spread, 1.0))


ROWS = 8


def corr_kernel(rec_ref, tr_ref, scale_ref, out_ref):
    channels, width = rec_ref.shape
    lag = tr_ref.shape[2]
    members, samples = out_ref.shape
    parts = tr_ref.shape[1] // members
    span = samples + parts * lag
    odd_width = samples + 2 * lag

    def one_group(g, carry):
        even_acc, odd_acc = carry
        first = pl.multiple_of(g * ROWS, ROWS)
        rows = rec_ref[pl.ds(first, ROWS), :]
        even_factors = scale_ref[pl.ds(first, ROWS), :]
        blank = jnp.zeros((ROWS, 2 * lag), jnp.float32)
        odd_factors = pltpu.roll(jnp.concatenate([even_factors, blank], axis=1), lag, 1)
        for r in range(ROWS):
            wide = jnp.broadcast_to(rows[r : r + 1, :], (lag, width))
            hankel = pltpu.roll(wide, width - (lag - 1), 1, stride=1, stride_axis=0)
            hankel = hankel[:, :span].astype(jnp.bfloat16)
            prod = jnp.dot(tr_ref[first + r], hankel, preferred_element_type=jnp.float32)
            even = prod[0:members, 0:samples]
            odd = prod[members : 2 * members, 0:odd_width]
            for i in range(1, parts // 2):
                lo = 2 * i * members
                even = even + prod[lo : lo + members, 2 * i * lag : 2 * i * lag + samples]
                odd = odd + prod[lo + members : lo + 2 * members, 2 * i * lag : 2 * i * lag + odd_width]
            even_acc = even_acc + even * even_factors[r : r + 1, :]
            odd_acc = odd_acc + odd * odd_factors[r : r + 1, :]
        return even_acc, odd_acc

    start = (
        jnp.zeros((members, samples), jnp.float32),
        jnp.zeros((members, odd_width), jnp.float32),
    )
    even_acc, odd_acc = lax.fori_loop(0, channels // ROWS, one_group, start)
    out_ref[...] = (even_acc + odd_acc[:, lag : lag + samples]) / channels


def lag_kernels(normalized):
    members, channels, window = normalized.shape
    parts = window // LAG_BLOCK
    kernels = normalized.reshape(members, channels, parts, LAG_BLOCK)[..., ::-1]
    return jnp.transpose(kernels, (1, 2, 0, 3)).reshape(channels, parts * members, LAG_BLOCK)


def stacked_correlation(extended, kernels, window, outputs):
    members = kernels.shape[1] * LAG_BLOCK // window
    scale = window_scale(extended, window, outputs)
    return pl.pallas_call(
        corr_kernel,
        out_shape=jax.ShapeDtypeStruct((members, outputs), jnp.float32),
    )(extended, kernels, scale)


def seg_sum(value):
    nseg = lax.axis_size("seg")
    copies = jnp.broadcast_to(value[None], (nseg,) + value.shape)
    return jnp.sum(lax.all_to_all(copies, "seg", 0, 0, tiled=True), axis=0)


def body(record, templates):
    channels, samples = record.shape
    window = templates.shape[2]
    nblk = lax.axis_size(BLK)
    group = gather_group(record)
    head = next_group_head(group, samples)
    kernels = lag_kernels(normalize(templates))
    inner = group.shape[1] - samples
    early = stacked_correlation(group, kernels, window, inner)
    tail = jnp.concatenate([group[:, inner:], head], axis=1)
    late = stacked_correlation(tail, kernels, window, samples)
    stacked = jnp.concatenate([early, late], axis=1)
    power_sum = seg_sum(jnp.sum(stacked * stacked, axis=1))
    record_len = samples * lax.axis_size("seg") * nblk
    detection = stacked / jnp.sqrt(power_sum / record_len + 1e-06)[:, None]
    members = detection.shape[0]
    pieces = detection.reshape(members, nblk, samples)
    spread = lax.all_to_all(pieces, BLK, 1, 0, tiled=True)
    return spread.reshape(members * nblk, samples)


BLK = ("bx", "bz")


def solution(mesh):
    nseg, nblk = mesh.shape["seg"], mesh.shape["blk"]
    split = Mesh(np.asarray(mesh.devices).reshape(nseg, nblk // 2, 2), ("seg",) + BLK)
    return jax.shard_map(
        body,
        mesh=split,
        in_specs=(P(None, ("seg",) + BLK), P(BLK, None, None)),
        out_specs=P(None, ("seg",) + BLK),
        check_vma=False,
    )
```

```python
import jax
import jax.numpy as jnp
from jax import lax
from jax.experimental import pallas as pl
from jax.experimental.pallas import tpu as pltpu
import numpy as np
from jax.sharding import Mesh, PartitionSpec as P

LAG_BLOCK = 64


def normalize(templates):
    widened = templates.astype(jnp.float32)
    centred = widened - jnp.mean(widened, axis=2, keepdims=True)
    return (centred / jnp.sqrt(jnp.sum(centred * centred, axis=2, keepdims=True) + 1e-06)).astype(
        jnp.bfloat16
    )


def gather_group(record):
    partner = lax.ppermute(record, "bz", [(0, 1), (1, 0)])
    low = lax.axis_index("bz") == 0
    pair = jnp.where(low, jnp.concatenate([record, partner], axis=1), jnp.concatenate([partner, record], axis=1))
    size = lax.axis_size("bx")
    channels, width = pair.shape
    copies = jnp.broadcast_to(pair[None], (size, channels, width))
    group = lax.all_to_all(copies, "bx", 0, 0, tiled=True)
    return jnp.transpose(group, (1, 0, 2)).reshape(channels, size * width)


def next_group_head(group, samples):
    nseg = lax.axis_size("seg")
    return lax.ppermute(group[:, :samples], "seg", [(i + 1, i) for i in range(nseg - 1)])


ROWS = 8


def window_sums(values, window, samples):
    width = values.shape[1]
    total = values
    step = 1
    while step < window:
        total = total + pltpu.roll(total, width - step, 1)
        step *= 2
    return total[:, :samples]


def corr_kernel(rec_ref, tr_ref, out_ref):
    channels, width = rec_ref.shape
    lag = tr_ref.shape[2]
    members, samples = out_ref.shape
    parts = tr_ref.shape[1] // members
    window = parts * lag
    span = samples + parts * lag
    odd_width = samples + 2 * lag

    def one_group(g, carry):
        even_acc, odd_acc = carry
        first = pl.multiple_of(g * ROWS, ROWS)
        rows = rec_ref[pl.ds(first, ROWS), :]
        window_sum = window_sums(rows, window, samples)
        window_sq = window_sums(rows * rows, window, samples)
        spread = window_sq - window_sum * window_sum / window
        even_factors = 1.0 / jnp.sqrt(jnp.maximum(spread, 1.0))
        blank = jnp.zeros((ROWS, 2 * lag), jnp.float32)
        odd_factors = pltpu.roll(jnp.concatenate([even_factors, blank], axis=1), lag, 1)
        for r in range(ROWS):
            wide = jnp.broadcast_to(rows[r : r + 1, :], (lag, width))
            hankel = pltpu.roll(wide, width - (lag - 1), 1, stride=1, stride_axis=0)
            hankel = hankel[:, :span].astype(jnp.bfloat16)
            prod = jnp.dot(tr_ref[first + r], hankel, preferred_element_type=jnp.float32)
            even = prod[0:members, 0:samples]
            odd = prod[members : 2 * members, 0:odd_width]
            for i in range(1, parts // 2):
                lo = 2 * i * members
                even = even + prod[lo : lo + members, 2 * i * lag : 2 * i * lag + samples]
                odd = odd + prod[lo + members : lo + 2 * members, 2 * i * lag : 2 * i * lag + odd_width]
            even_acc = even_acc + even * even_factors[r : r + 1, :]
            odd_acc = odd_acc + odd * odd_factors[r : r + 1, :]
        return even_acc, odd_acc

    start = (
        jnp.zeros((members, samples), jnp.float32),
        jnp.zeros((members, odd_width), jnp.float32),
    )
    even_acc, odd_acc = lax.fori_loop(0, channels // ROWS, one_group, start)
    out_ref[...] = (even_acc + odd_acc[:, lag : lag + samples]) / channels


def lag_kernels(normalized):
    members, channels, window = normalized.shape
    parts = window // LAG_BLOCK
    kernels = normalized.reshape(members, channels, parts, LAG_BLOCK)[..., ::-1]
    return jnp.transpose(kernels, (1, 2, 0, 3)).reshape(channels, parts * members, LAG_BLOCK)


def stacked_correlation(extended, kernels, window, outputs):
    members = kernels.shape[1] * LAG_BLOCK // window
    return pl.pallas_call(
        corr_kernel,
        out_shape=jax.ShapeDtypeStruct((members, outputs), jnp.float32),
    )(extended, kernels)


def seg_sum(value):
    nseg = lax.axis_size("seg")
    copies = jnp.broadcast_to(value[None], (nseg,) + value.shape)
    return jnp.sum(lax.all_to_all(copies, "seg", 0, 0, tiled=True), axis=0)


def body(record, templates):
    channels, samples = record.shape
    window = templates.shape[2]
    nblk = lax.axis_size(BLK)
    group = gather_group(record)
    head = next_group_head(group, samples)
    kernels = lag_kernels(normalize(templates))
    inner = group.shape[1] - samples
    early = stacked_correlation(group, kernels, window, inner)
    tail = jnp.concatenate([group[:, inner:], head], axis=1)
    late = stacked_correlation(tail, kernels, window, samples)
    stacked = jnp.concatenate([early, late], axis=1)
    power_sum = seg_sum(jnp.sum(stacked * stacked, axis=1))
    record_len = samples * lax.axis_size("seg") * nblk
    detection = stacked / jnp.sqrt(power_sum / record_len + 1e-06)[:, None]
    members = detection.shape[0]
    pieces = detection.reshape(members, nblk, samples)
    spread = lax.all_to_all(pieces, BLK, 1, 0, tiled=True)
    return spread.reshape(members * nblk, samples)


BLK = ("bx", "bz")


def solution(mesh):
    nseg, nblk = mesh.shape["seg"], mesh.shape["blk"]
    split = Mesh(np.asarray(mesh.devices).reshape(nseg, nblk // 2, 2), ("seg",) + BLK)
    return jax.shard_map(
        body,
        mesh=split,
        in_specs=(P(None, ("seg",) + BLK), P(BLK, None, None)),
        out_specs=P(None, ("seg",) + BLK),
        check_vma=False,
    )
```

```python
import jax
import jax.numpy as jnp
from jax import lax
from jax.experimental import pallas as pl
from jax.experimental.pallas import tpu as pltpu
import numpy as np
from jax.sharding import Mesh, PartitionSpec as P

LAG_BLOCK = 64


def gather_group(record):
    partner = lax.ppermute(record, "bz", [(0, 1), (1, 0)])
    low = lax.axis_index("bz") == 0
    pair = jnp.where(low, jnp.concatenate([record, partner], axis=1), jnp.concatenate([partner, record], axis=1))
    size = lax.axis_size("bx")
    channels, width = pair.shape
    copies = jnp.broadcast_to(pair[None], (size, channels, width))
    group = lax.all_to_all(copies, "bx", 0, 0, tiled=True)
    return jnp.transpose(group, (1, 0, 2)).reshape(channels, size * width)


def next_group_head(group, samples):
    nseg = lax.axis_size("seg")
    return lax.ppermute(group[:, :samples], "seg", [(i + 1, i) for i in range(nseg - 1)])


ROWS = 8


def window_sums(values, window, samples):
    width = values.shape[1]
    total = values
    step = 1
    while step < window:
        total = total + pltpu.roll(total, width - step, 1)
        step *= 2
    return total[:, :samples]


def corr_kernel(rec_ref, tr_ref, out_ref):
    channels, width = rec_ref.shape
    lag = tr_ref.shape[2]
    members, samples = out_ref.shape
    parts = tr_ref.shape[1] // members
    window = parts * lag
    span = samples + parts * lag
    odd_width = samples + 2 * lag

    def one_group(g, carry):
        even_acc, odd_acc = carry
        first = pl.multiple_of(g * ROWS, ROWS)
        rows = rec_ref[pl.ds(first, ROWS), :]
        window_sum = window_sums(rows, window, samples)
        window_sq = window_sums(rows * rows, window, samples)
        spread = window_sq - window_sum * window_sum / window
        even_factors = 1.0 / jnp.sqrt(jnp.maximum(spread, 1.0))
        blank = jnp.zeros((ROWS, 2 * lag), jnp.float32)
        odd_factors = pltpu.roll(jnp.concatenate([even_factors, blank], axis=1), lag, 1)
        for r in range(ROWS):
            wide = jnp.broadcast_to(rows[r : r + 1, :], (lag, width))
            hankel = pltpu.roll(wide, width - (lag - 1), 1, stride=1, stride_axis=0)
            hankel = hankel[:, :span].astype(jnp.bfloat16)
            prod = jnp.dot(tr_ref[first + r], hankel, preferred_element_type=jnp.float32)
            even = prod[0:members, 0:samples]
            odd = prod[members : 2 * members, 0:odd_width]
            for i in range(1, parts // 2):
                lo = 2 * i * members
                even = even + prod[lo : lo + members, 2 * i * lag : 2 * i * lag + samples]
                odd = odd + prod[lo + members : lo + 2 * members, 2 * i * lag : 2 * i * lag + odd_width]
            even_acc = even_acc + even * even_factors[r : r + 1, :]
            odd_acc = odd_acc + odd * odd_factors[r : r + 1, :]
        return even_acc, odd_acc

    start = (
        jnp.zeros((members, samples), jnp.float32),
        jnp.zeros((members, odd_width), jnp.float32),
    )
    even_acc, odd_acc = lax.fori_loop(0, channels // ROWS, one_group, start)
    out_ref[...] = (even_acc + odd_acc[:, lag : lag + samples]) / channels


def lag_kernels(templates):
    members, channels, window = templates.shape
    parts = window // LAG_BLOCK
    laid = templates.reshape(members, channels, parts, LAG_BLOCK)[..., ::-1]
    laid = jnp.transpose(laid, (1, 2, 0, 3)).astype(jnp.float32)
    centred = laid - jnp.mean(laid, axis=(1, 3), keepdims=True)
    norm = jnp.sqrt(jnp.sum(centred * centred, axis=(1, 3), keepdims=True) + 1e-06)
    return (centred / norm).astype(jnp.bfloat16).reshape(channels, parts * members, LAG_BLOCK)


def stacked_correlation(extended, kernels, window, outputs):
    members = kernels.shape[1] * LAG_BLOCK // window
    return pl.pallas_call(
        corr_kernel,
        out_shape=jax.ShapeDtypeStruct((members, outputs), jnp.float32),
    )(extended, kernels)


def seg_sum(value):
    nseg = lax.axis_size("seg")
    copies = jnp.broadcast_to(value[None], (nseg,) + value.shape)
    return jnp.sum(lax.all_to_all(copies, "seg", 0, 0, tiled=True), axis=0)


def body(record, templates):
    channels, samples = record.shape
    window = templates.shape[2]
    nblk = lax.axis_size(BLK)
    group = gather_group(record)
    head = next_group_head(group, samples)
    kernels = lag_kernels(templates)
    inner = group.shape[1] - samples
    early = stacked_correlation(group, kernels, window, inner)
    tail = jnp.concatenate([group[:, inner:], head], axis=1)
    late = stacked_correlation(tail, kernels, window, samples)
    stacked = jnp.concatenate([early, late], axis=1)
    power_sum = seg_sum(jnp.sum(stacked * stacked, axis=1))
    record_len = samples * lax.axis_size("seg") * nblk
    detection = stacked / jnp.sqrt(power_sum / record_len + 1e-06)[:, None]
    members = detection.shape[0]
    pieces = detection.reshape(members, nblk, samples)
    spread = lax.all_to_all(pieces, BLK, 1, 0, tiled=True)
    return spread.reshape(members * nblk, samples)


BLK = ("bx", "bz")


def solution(mesh):
    nseg, nblk = mesh.shape["seg"], mesh.shape["blk"]
    split = Mesh(np.asarray(mesh.devices).reshape(nseg, nblk // 2, 2), ("seg",) + BLK)
    return jax.shard_map(
        body,
        mesh=split,
        in_specs=(P(None, ("seg",) + BLK), P(BLK, None, None)),
        out_specs=P(None, ("seg",) + BLK),
        check_vma=False,
    )
```

```python
import jax
import jax.numpy as jnp
from jax import lax
from jax.experimental import pallas as pl
from jax.experimental.pallas import tpu as pltpu
import numpy as np
from jax.sharding import Mesh, PartitionSpec as P

LAG_BLOCK = 64


def gather_group(record):
    partner = lax.ppermute(record, "bz", [(0, 1), (1, 0)])
    low = lax.axis_index("bz") == 0
    pair = jnp.where(low, jnp.concatenate([record, partner], axis=1), jnp.concatenate([partner, record], axis=1))
    size = lax.axis_size("bx")
    channels, width = pair.shape
    copies = jnp.broadcast_to(pair[None], (size, channels, width))
    group = lax.all_to_all(copies, "bx", 0, 0, tiled=True)
    return jnp.transpose(group, (1, 0, 2)).reshape(channels, size * width)


def next_group_head(group, samples):
    nseg = lax.axis_size("seg")
    return lax.ppermute(group[:, :samples], "seg", [(i + 1, i) for i in range(nseg - 1)])


ROWS = 8


def window_sums(values, window, samples):
    width = values.shape[1]
    total = values
    step = 1
    while step < window:
        total = total + pltpu.roll(total, width - step, 1)
        step *= 2
    return total[:, :samples]


def corr_kernel(rec_ref, tr_ref, out_ref):
    channels, width = rec_ref.shape
    lag = tr_ref.shape[2]
    members, samples = out_ref.shape
    parts = tr_ref.shape[1] // members
    window = parts * lag
    span = samples + parts * lag
    odd_width = samples + 2 * lag

    def one_group(g, carry):
        even_acc, odd_acc = carry
        first = pl.multiple_of(g * ROWS, ROWS)
        rows = rec_ref[pl.ds(first, ROWS), :]
        window_sum = window_sums(rows, window, samples)
        window_sq = window_sums(rows * rows, window, samples)
        spread = window_sq - window_sum * window_sum / window
        even_factors = 1.0 / jnp.sqrt(jnp.maximum(spread, 1.0))
        blank = jnp.zeros((ROWS, 2 * lag), jnp.float32)
        odd_factors = pltpu.roll(jnp.concatenate([even_factors, blank], axis=1), lag, 1)
        for r in range(ROWS):
            wide = jnp.broadcast_to(rows[r : r + 1, :], (lag, width))
            hankel = pltpu.roll(wide, width - (lag - 1), 1, stride=1, stride_axis=0)
            hankel = hankel[:, :span].astype(jnp.bfloat16)
            prod = jnp.dot(tr_ref[first + r], hankel, preferred_element_type=jnp.float32)
            even = prod[0:members, 0:samples]
            odd = prod[members : 2 * members, 0:odd_width]
            for i in range(1, parts // 2):
                lo = 2 * i * members
                even = even + prod[lo : lo + members, 2 * i * lag : 2 * i * lag + samples]
                odd = odd + prod[lo + members : lo + 2 * members, 2 * i * lag : 2 * i * lag + odd_width]
            even_acc = even_acc + even * even_factors[r : r + 1, :]
            odd_acc = odd_acc + odd * odd_factors[r : r + 1, :]
        return even_acc, odd_acc

    start = (
        jnp.zeros((members, samples), jnp.float32),
        jnp.zeros((members, odd_width), jnp.float32),
    )
    even_acc, odd_acc = lax.fori_loop(0, channels // ROWS, one_group, start)
    out_ref[...] = (even_acc + odd_acc[:, lag : lag + samples]) / channels


def lag_kernels(templates):
    members, channels, window = templates.shape
    parts = window // LAG_BLOCK
    laid = templates.reshape(members, channels, parts, LAG_BLOCK)[..., ::-1]
    laid = jnp.transpose(laid, (1, 2, 0, 3)).astype(jnp.float32)
    centred = laid - jnp.mean(laid, axis=(1, 3), keepdims=True)
    norm = jnp.sqrt(jnp.sum(centred * centred, axis=(1, 3), keepdims=True) + 1e-06)
    return (centred / norm).astype(jnp.bfloat16).reshape(channels, parts * members, LAG_BLOCK)


def stacked_correlation(extended, kernels, window, outputs):
    members = kernels.shape[1] * LAG_BLOCK // window
    return pl.pallas_call(
        corr_kernel,
        out_shape=jax.ShapeDtypeStruct((members, outputs), jnp.float32),
    )(extended, kernels)


def seg_sum(value):
    nseg = lax.axis_size("seg")
    copies = jnp.broadcast_to(value[None], (nseg,) + value.shape)
    return jnp.sum(lax.all_to_all(copies, "seg", 0, 0, tiled=True), axis=0)


def body(record, templates):
    channels, samples = record.shape
    window = templates.shape[2]
    nblk = lax.axis_size(BLK)
    group = gather_group(record)
    head = next_group_head(group, samples)
    kernels = lag_kernels(templates)
    inner = group.shape[1] - samples
    early = stacked_correlation(group, kernels, window, inner)
    tail = jnp.concatenate([group[:, inner:], head], axis=1)
    late = stacked_correlation(tail, kernels, window, samples)
    stacked = jnp.concatenate([early, late], axis=1)
    power_sum = seg_sum(jnp.sum(stacked * stacked, axis=1))
    record_len = samples * lax.axis_size("seg") * nblk
    detection = stacked / jnp.sqrt(power_sum / record_len + 1e-06)[:, None]
    members = detection.shape[0]
    pieces = detection.reshape(members, nblk // 2, 2, samples)
    near = lax.all_to_all(pieces, "bx", 1, 1, tiled=True)
    side = lax.axis_index("bz")
    own = lax.dynamic_index_in_dim(near, side, axis=2, keepdims=False)
    other = lax.dynamic_index_in_dim(near, 1 - side, axis=2, keepdims=False)
    far = lax.ppermute(other, "bz", [(0, 1), (1, 0)])
    low = side == 0
    both = jnp.where(low, jnp.stack([own, far], axis=2), jnp.stack([far, own], axis=2))
    return jnp.transpose(both, (1, 2, 0, 3)).reshape(members * nblk, samples)


BLK = ("bx", "bz")


def solution(mesh):
    nseg, nblk = mesh.shape["seg"], mesh.shape["blk"]
    split = Mesh(np.asarray(mesh.devices).reshape(nseg, nblk // 2, 2), ("seg",) + BLK)
    return jax.shard_map(
        body,
        mesh=split,
        in_specs=(P(None, ("seg",) + BLK), P(BLK, None, None)),
        out_specs=P(None, ("seg",) + BLK),
        check_vma=False,
    )
```

```python
import jax
import jax.numpy as jnp
from jax import lax
from jax.experimental import pallas as pl
from jax.experimental.pallas import tpu as pltpu
import numpy as np
from jax.sharding import Mesh, PartitionSpec as P

LAG_BLOCK = 64


def gather_group(record):
    partner = lax.ppermute(record, "bz", [(0, 1), (1, 0)])
    low = lax.axis_index("bz") == 0
    pair = jnp.where(low, jnp.concatenate([record, partner], axis=1), jnp.concatenate([partner, record], axis=1))
    size = lax.axis_size("bx")
    channels, width = pair.shape
    copies = jnp.broadcast_to(pair[None], (size, channels, width))
    group = lax.all_to_all(copies, "bx", 0, 0, tiled=True)
    return jnp.transpose(group, (1, 0, 2)).reshape(channels, size * width)


def next_group_head(group, samples):
    nseg = lax.axis_size("seg")
    return lax.ppermute(group[:, :samples], "seg", [(i + 1, i) for i in range(nseg - 1)])


ROWS = 8


def window_sums(values, window, samples):
    width = values.shape[1]
    total = values
    step = 1
    while step < window:
        total = total + pltpu.roll(total, width - step, 1)
        step *= 2
    return total[:, :samples]


def corr_kernel(rec_ref, tr_ref, out_ref):
    channels, width = rec_ref.shape
    lag = tr_ref.shape[2]
    members, samples = out_ref.shape
    parts = tr_ref.shape[1] // members
    window = parts * lag
    span = samples + parts * lag
    odd_width = samples + 2 * lag

    def one_group(g, carry):
        even_acc, odd_acc = carry
        first = pl.multiple_of(g * ROWS, ROWS)
        rows = rec_ref[pl.ds(first, ROWS), :]
        window_sum = window_sums(rows, window, samples)
        window_sq = window_sums(rows * rows, window, samples)
        spread = window_sq - window_sum * window_sum / window
        even_factors = 1.0 / jnp.sqrt(jnp.maximum(spread, 1.0))
        blank = jnp.zeros((ROWS, 2 * lag), jnp.float32)
        odd_factors = pltpu.roll(jnp.concatenate([even_factors, blank], axis=1), lag, 1)
        for r in range(ROWS):
            wide = jnp.broadcast_to(rows[r : r + 1, :], (lag, width))
            hankel = pltpu.roll(wide, width - (lag - 1), 1, stride=1, stride_axis=0)
            hankel = hankel[:, :span].astype(jnp.bfloat16)
            prod = jnp.dot(tr_ref[first + r], hankel, preferred_element_type=jnp.float32)
            even = prod[0:members, 0:samples]
            odd = prod[members : 2 * members, 0:odd_width]
            for i in range(1, parts // 2):
                lo = 2 * i * members
                even = even + prod[lo : lo + members, 2 * i * lag : 2 * i * lag + samples]
                odd = odd + prod[lo + members : lo + 2 * members, 2 * i * lag : 2 * i * lag + odd_width]
            even_acc = even_acc + even * even_factors[r : r + 1, :]
            odd_acc = odd_acc + odd * odd_factors[r : r + 1, :]
        return even_acc, odd_acc

    start = (
        jnp.zeros((members, samples), jnp.float32),
        jnp.zeros((members, odd_width), jnp.float32),
    )
    even_acc, odd_acc = lax.fori_loop(0, channels // ROWS, one_group, start, unroll=True)
    out_ref[...] = (even_acc + odd_acc[:, lag : lag + samples]) / channels


def lag_kernels(templates):
    members, channels, window = templates.shape
    parts = window // LAG_BLOCK
    laid = templates.reshape(members, channels, parts, LAG_BLOCK)[..., ::-1]
    laid = jnp.transpose(laid, (1, 2, 0, 3)).astype(jnp.float32)
    centred = laid - jnp.mean(laid, axis=(1, 3), keepdims=True)
    norm = jnp.sqrt(jnp.sum(centred * centred, axis=(1, 3), keepdims=True) + 1e-06)
    return (centred / norm).astype(jnp.bfloat16).reshape(channels, parts * members, LAG_BLOCK)


def stacked_correlation(extended, kernels, window, outputs):
    members = kernels.shape[1] * LAG_BLOCK // window
    return pl.pallas_call(
        corr_kernel,
        out_shape=jax.ShapeDtypeStruct((members, outputs), jnp.float32),
    )(extended, kernels)


def seg_sum(value):
    nseg = lax.axis_size("seg")
    copies = jnp.broadcast_to(value[None], (nseg,) + value.shape)
    return jnp.sum(lax.all_to_all(copies, "seg", 0, 0, tiled=True), axis=0)


def body(record, templates):
    channels, samples = record.shape
    window = templates.shape[2]
    nblk = lax.axis_size(BLK)
    group = gather_group(record)
    head = next_group_head(group, samples)
    kernels = lag_kernels(templates)
    inner = group.shape[1] - samples
    early = stacked_correlation(group, kernels, window, inner)
    tail = jnp.concatenate([group[:, inner:], head], axis=1)
    late = stacked_correlation(tail, kernels, window, samples)
    stacked = jnp.concatenate([early, late], axis=1)
    power_sum = seg_sum(jnp.sum(stacked * stacked, axis=1))
    record_len = samples * lax.axis_size("seg") * nblk
    detection = stacked / jnp.sqrt(power_sum / record_len + 1e-06)[:, None]
    members = detection.shape[0]
    pieces = detection.reshape(members, nblk, samples)
    spread = lax.all_to_all(pieces, BLK, 1, 0, tiled=True)
    return spread.reshape(members * nblk, samples)


BLK = ("bx", "bz")


def solution(mesh):
    nseg, nblk = mesh.shape["seg"], mesh.shape["blk"]
    split = Mesh(np.asarray(mesh.devices).reshape(nseg, nblk // 2, 2), ("seg",) + BLK)
    return jax.shard_map(
        body,
        mesh=split,
        in_specs=(P(None, ("seg",) + BLK), P(BLK, None, None)),
        out_specs=P(None, ("seg",) + BLK),
        check_vma=False,
    )
```

```python
import jax
import jax.numpy as jnp
from jax import lax
from jax.experimental import pallas as pl
from jax.experimental.pallas import tpu as pltpu
import numpy as np
from jax.sharding import Mesh, PartitionSpec as P

LAG_BLOCK = 64


def gather_group(record):
    partner = lax.ppermute(record, "bz", [(0, 1), (1, 0)])
    low = lax.axis_index("bz") == 0
    pair = jnp.where(low, jnp.concatenate([record, partner], axis=1), jnp.concatenate([partner, record], axis=1))
    size = lax.axis_size("bx")
    channels, width = pair.shape
    copies = jnp.broadcast_to(pair[None], (size, channels, width))
    return lax.all_to_all(copies, "bx", 0, 0, tiled=True)


def next_group_head(group, samples):
    nseg = lax.axis_size("seg")
    return lax.ppermute(group[:, :samples], "seg", [(i + 1, i) for i in range(nseg - 1)])


ROWS = 8


def window_sums(values, window, samples):
    width = values.shape[1]
    total = values
    step = 1
    while step < window:
        total = total + pltpu.roll(total, width - step, 1)
        step *= 2
    return total[:, :samples]


def corr_kernel(load_rows, channels, width, tr_ref, out_ref):
    lag = tr_ref.shape[2]
    members, samples = out_ref.shape
    parts = tr_ref.shape[1] // members
    window = parts * lag
    span = samples + parts * lag
    odd_width = samples + 2 * lag

    def one_group(g, carry):
        even_acc, odd_acc = carry
        first = pl.multiple_of(g * ROWS, ROWS)
        rows = load_rows(first)
        window_sum = window_sums(rows, window, samples)
        window_sq = window_sums(rows * rows, window, samples)
        spread = window_sq - window_sum * window_sum / window
        even_factors = 1.0 / jnp.sqrt(jnp.maximum(spread, 1.0))
        blank = jnp.zeros((ROWS, 2 * lag), jnp.float32)
        odd_factors = pltpu.roll(jnp.concatenate([even_factors, blank], axis=1), lag, 1)
        for r in range(ROWS):
            wide = jnp.broadcast_to(rows[r : r + 1, :], (lag, width))
            hankel = pltpu.roll(wide, width - (lag - 1), 1, stride=1, stride_axis=0)
            hankel = hankel[:, :span].astype(jnp.bfloat16)
            prod = jnp.dot(tr_ref[first + r], hankel, preferred_element_type=jnp.float32)
            even = prod[0:members, 0:samples]
            odd = prod[members : 2 * members, 0:odd_width]
            for i in range(1, parts // 2):
                lo = 2 * i * members
                even = even + prod[lo : lo + members, 2 * i * lag : 2 * i * lag + samples]
                odd = odd + prod[lo + members : lo + 2 * members, 2 * i * lag : 2 * i * lag + odd_width]
            even_acc = even_acc + even * even_factors[r : r + 1, :]
            odd_acc = odd_acc + odd * odd_factors[r : r + 1, :]
        return even_acc, odd_acc

    start = (
        jnp.zeros((members, samples), jnp.float32),
        jnp.zeros((members, odd_width), jnp.float32),
    )
    even_acc, odd_acc = lax.fori_loop(0, channels // ROWS, one_group, start, unroll=True)
    out_ref[...] = (even_acc + odd_acc[:, lag : lag + samples]) / channels


def lag_kernels(templates):
    members, channels, window = templates.shape
    parts = window // LAG_BLOCK
    laid = templates.reshape(members, channels, parts, LAG_BLOCK)[..., ::-1]
    laid = jnp.transpose(laid, (1, 2, 0, 3)).astype(jnp.float32)
    centred = laid - jnp.mean(laid, axis=(1, 3), keepdims=True)
    norm = jnp.sqrt(jnp.sum(centred * centred, axis=(1, 3), keepdims=True) + 1e-06)
    return (centred / norm).astype(jnp.bfloat16).reshape(channels, parts * members, LAG_BLOCK)


def early_kernel(group_ref, tr_ref, out_ref):
    pairs, channels, width = group_ref.shape

    def load_rows(first):
        return jnp.concatenate([group_ref[m, pl.ds(first, ROWS), :] for m in range(pairs)], axis=1)

    corr_kernel(load_rows, channels, pairs * width, tr_ref, out_ref)


def late_kernel(group_ref, head_ref, tr_ref, out_ref):
    pairs, channels, width = group_ref.shape
    samples = head_ref.shape[1]

    def load_rows(first):
        last = group_ref[pairs - 1, pl.ds(first, ROWS), :]
        return jnp.concatenate([last[:, width - samples :], head_ref[pl.ds(first, ROWS), :]], axis=1)

    corr_kernel(load_rows, channels, 2 * samples, tr_ref, out_ref)


def stacked_correlation(group, head, kernels, window):
    pairs, channels, width = group.shape
    samples = head.shape[1]
    members = kernels.shape[1] * LAG_BLOCK // window
    early = pl.pallas_call(
        early_kernel,
        out_shape=jax.ShapeDtypeStruct((members, pairs * width - samples), jnp.float32),
    )(group, kernels)
    late = pl.pallas_call(
        late_kernel,
        out_shape=jax.ShapeDtypeStruct((members, samples), jnp.float32),
    )(group, head, kernels)
    return jnp.concatenate([early, late], axis=1)


def seg_sum(value):
    nseg = lax.axis_size("seg")
    copies = jnp.broadcast_to(value[None], (nseg,) + value.shape)
    return jnp.sum(lax.all_to_all(copies, "seg", 0, 0, tiled=True), axis=0)


def body(record, templates):
    channels, samples = record.shape
    window = templates.shape[2]
    nblk = lax.axis_size(BLK)
    group = gather_group(record)
    head = next_group_head(group[0], samples)
    kernels = lag_kernels(templates)
    stacked = stacked_correlation(group, head, kernels, window)
    power_sum = seg_sum(jnp.sum(stacked * stacked, axis=1))
    record_len = samples * lax.axis_size("seg") * nblk
    detection = stacked / jnp.sqrt(power_sum / record_len + 1e-06)[:, None]
    members = detection.shape[0]
    pieces = detection.reshape(members, nblk, samples)
    spread = lax.all_to_all(pieces, BLK, 1, 0, tiled=True)
    return spread.reshape(members * nblk, samples)


BLK = ("bx", "bz")


def solution(mesh):
    nseg, nblk = mesh.shape["seg"], mesh.shape["blk"]
    split = Mesh(np.asarray(mesh.devices).reshape(nseg, nblk // 2, 2), ("seg",) + BLK)
    return jax.shard_map(
        body,
        mesh=split,
        in_specs=(P(None, ("seg",) + BLK), P(BLK, None, None)),
        out_specs=P(None, ("seg",) + BLK),
        check_vma=False,
    )
```

```python
import jax
import jax.numpy as jnp
from jax import lax
from jax.experimental import pallas as pl
from jax.experimental.pallas import tpu as pltpu
import numpy as np
from jax.sharding import Mesh, PartitionSpec as P

LAG_BLOCK = 64


def gather_group(record, kernels):
    partner = lax.ppermute(record, "bz", [(0, 1), (1, 0)])
    low = lax.axis_index("bz") == 0
    pair = jnp.where(low, jnp.concatenate([record, partner], axis=1), jnp.concatenate([partner, record], axis=1))
    pair, kernels = lax.optimization_barrier((pair, kernels))
    size = lax.axis_size("bx")
    channels, width = pair.shape
    copies = jnp.broadcast_to(pair[None], (size, channels, width))
    return lax.all_to_all(copies, "bx", 0, 0, tiled=True), kernels


def next_group_head(group, samples):
    nseg = lax.axis_size("seg")
    return lax.ppermute(group[:, :samples], "seg", [(i + 1, i) for i in range(nseg - 1)])


ROWS = 8


def window_sums(values, window, samples):
    width = values.shape[1]
    total = values
    step = 1
    while step < window:
        total = total + pltpu.roll(total, width - step, 1)
        step *= 2
    return total[:, :samples]


def corr_kernel(load_rows, channels, width, tr_ref, out_ref):
    lag = tr_ref.shape[2]
    members, samples = out_ref.shape
    parts = tr_ref.shape[1] // members
    window = parts * lag
    span = samples + parts * lag
    odd_width = samples + 2 * lag

    def one_group(g, carry):
        even_acc, odd_acc = carry
        first = pl.multiple_of(g * ROWS, ROWS)
        rows = load_rows(first)
        window_sum = window_sums(rows, window, samples)
        window_sq = window_sums(rows * rows, window, samples)
        spread = window_sq - window_sum * window_sum / window
        even_factors = 1.0 / jnp.sqrt(jnp.maximum(spread, 1.0))
        blank = jnp.zeros((ROWS, 2 * lag), jnp.float32)
        odd_factors = pltpu.roll(jnp.concatenate([even_factors, blank], axis=1), lag, 1)
        for r in range(ROWS):
            wide = jnp.broadcast_to(rows[r : r + 1, :], (lag, width))
            hankel = pltpu.roll(wide, width - (lag - 1), 1, stride=1, stride_axis=0)
            hankel = hankel[:, :span].astype(jnp.bfloat16)
            prod = jnp.dot(tr_ref[first + r], hankel, preferred_element_type=jnp.float32)
            even = prod[0:members, 0:samples]
            odd = prod[members : 2 * members, 0:odd_width]
            for i in range(1, parts // 2):
                lo = 2 * i * members
                even = even + prod[lo : lo + members, 2 * i * lag : 2 * i * lag + samples]
                odd = odd + prod[lo + members : lo + 2 * members, 2 * i * lag : 2 * i * lag + odd_width]
            even_acc = even_acc + even * even_factors[r : r + 1, :]
            odd_acc = odd_acc + odd * odd_factors[r : r + 1, :]
        return even_acc, odd_acc

    start = (
        jnp.zeros((members, samples), jnp.float32),
        jnp.zeros((members, odd_width), jnp.float32),
    )
    even_acc, odd_acc = lax.fori_loop(0, channels // ROWS, one_group, start, unroll=True)
    out_ref[...] = (even_acc + odd_acc[:, lag : lag + samples]) / channels


def lag_kernels(templates):
    members, channels, window = templates.shape
    parts = window // LAG_BLOCK
    laid = templates.reshape(members, channels, parts, LAG_BLOCK)[..., ::-1]
    laid = jnp.transpose(laid, (1, 2, 0, 3)).astype(jnp.float32)
    centred = laid - jnp.mean(laid, axis=(1, 3), keepdims=True)
    norm = jnp.sqrt(jnp.sum(centred * centred, axis=(1, 3), keepdims=True) + 1e-06)
    return (centred / norm).astype(jnp.bfloat16).reshape(channels, parts * members, LAG_BLOCK)


def early_kernel(group_ref, tr_ref, out_ref):
    pairs, channels, width = group_ref.shape

    def load_rows(first):
        return jnp.concatenate([group_ref[m, pl.ds(first, ROWS), :] for m in range(pairs)], axis=1)

    corr_kernel(load_rows, channels, pairs * width, tr_ref, out_ref)


def late_kernel(group_ref, head_ref, tr_ref, out_ref):
    pairs, channels, width = group_ref.shape
    samples = head_ref.shape[1]

    def load_rows(first):
        last = group_ref[pairs - 1, pl.ds(first, ROWS), :]
        return jnp.concatenate([last[:, width - samples :], head_ref[pl.ds(first, ROWS), :]], axis=1)

    corr_kernel(load_rows, channels, 2 * samples, tr_ref, out_ref)


def stacked_correlation(group, head, kernels, window):
    pairs, channels, width = group.shape
    samples = head.shape[1]
    members = kernels.shape[1] * LAG_BLOCK // window
    early = pl.pallas_call(
        early_kernel,
        out_shape=jax.ShapeDtypeStruct((members, pairs * width - samples), jnp.float32),
    )(group, kernels)
    late = pl.pallas_call(
        late_kernel,
        out_shape=jax.ShapeDtypeStruct((members, samples), jnp.float32),
    )(group, head, kernels)
    return jnp.concatenate([early, late], axis=1)


def seg_sum(value):
    nseg = lax.axis_size("seg")
    copies = jnp.broadcast_to(value[None], (nseg,) + value.shape)
    return jnp.sum(lax.all_to_all(copies, "seg", 0, 0, tiled=True), axis=0)


def body(record, templates):
    channels, samples = record.shape
    window = templates.shape[2]
    nblk = lax.axis_size(BLK)
    group, kernels = gather_group(record, lag_kernels(templates))
    head = next_group_head(group[0], samples)
    stacked = stacked_correlation(group, head, kernels, window)
    power_sum = seg_sum(jnp.sum(stacked * stacked, axis=1))
    record_len = samples * lax.axis_size("seg") * nblk
    detection = stacked / jnp.sqrt(power_sum / record_len + 1e-06)[:, None]
    members = detection.shape[0]
    pieces = detection.reshape(members, nblk, samples)
    spread = lax.all_to_all(pieces, BLK, 1, 0, tiled=True)
    return spread.reshape(members * nblk, samples)


BLK = ("bx", "bz")


def solution(mesh):
    nseg, nblk = mesh.shape["seg"], mesh.shape["blk"]
    split = Mesh(np.asarray(mesh.devices).reshape(nseg, nblk // 2, 2), ("seg",) + BLK)
    return jax.shard_map(
        body,
        mesh=split,
        in_specs=(P(None, ("seg",) + BLK), P(BLK, None, None)),
        out_specs=P(None, ("seg",) + BLK),
        check_vma=False,
    )
```

```python
import jax
import jax.numpy as jnp
from jax import lax
from jax.experimental import pallas as pl
from jax.experimental.pallas import tpu as pltpu
import numpy as np
from jax.sharding import Mesh, PartitionSpec as P

LAG_BLOCK = 64


def gather_group(record, kernels):
    partner = lax.ppermute(record, "bz", [(0, 1), (1, 0)])
    low = lax.axis_index("bz") == 0
    pair = jnp.where(low, jnp.concatenate([record, partner], axis=1), jnp.concatenate([partner, record], axis=1))
    pair, kernels = lax.optimization_barrier((pair, kernels))
    size = lax.axis_size("bx")
    channels, width = pair.shape
    copies = jnp.broadcast_to(pair[None], (size, channels, width))
    return lax.all_to_all(copies, "bx", 0, 0, tiled=True), kernels


def next_group_head(group, samples):
    nseg = lax.axis_size("seg")
    return lax.ppermute(group[:, :samples], "seg", [(i + 1, i) for i in range(nseg - 1)])


ROWS = 8


def window_sums(values, window, samples):
    width = values.shape[1]
    total = values
    step = 1
    while step < window:
        total = total + pltpu.roll(total, width - step, 1)
        step *= 2
    return total[:, :samples]


def corr_kernel(load_rows, channels, width, tr_ref, out_ref, power_ref):
    lag = tr_ref.shape[2]
    members, samples = out_ref.shape
    parts = tr_ref.shape[1] // members
    window = parts * lag
    span = samples + parts * lag
    odd_width = samples + 2 * lag

    def one_group(g, carry):
        even_acc, odd_acc = carry
        first = pl.multiple_of(g * ROWS, ROWS)
        rows = load_rows(first)
        window_sum = window_sums(rows, window, samples)
        window_sq = window_sums(rows * rows, window, samples)
        spread = window_sq - window_sum * window_sum / window
        even_factors = 1.0 / jnp.sqrt(jnp.maximum(spread, 1.0))
        blank = jnp.zeros((ROWS, 2 * lag), jnp.float32)
        odd_factors = pltpu.roll(jnp.concatenate([even_factors, blank], axis=1), lag, 1)
        for r in range(ROWS):
            wide = jnp.broadcast_to(rows[r : r + 1, :], (lag, width))
            hankel = pltpu.roll(wide, width - (lag - 1), 1, stride=1, stride_axis=0)
            hankel = hankel[:, :span].astype(jnp.bfloat16)
            prod = jnp.dot(tr_ref[first + r], hankel, preferred_element_type=jnp.float32)
            even = prod[0:members, 0:samples]
            odd = prod[members : 2 * members, 0:odd_width]
            for i in range(1, parts // 2):
                lo = 2 * i * members
                even = even + prod[lo : lo + members, 2 * i * lag : 2 * i * lag + samples]
                odd = odd + prod[lo + members : lo + 2 * members, 2 * i * lag : 2 * i * lag + odd_width]
            even_acc = even_acc + even * even_factors[r : r + 1, :]
            odd_acc = odd_acc + odd * odd_factors[r : r + 1, :]
        return even_acc, odd_acc

    start = (
        jnp.zeros((members, samples), jnp.float32),
        jnp.zeros((members, odd_width), jnp.float32),
    )
    even_acc, odd_acc = lax.fori_loop(0, channels // ROWS, one_group, start, unroll=True)
    stacked = (even_acc + odd_acc[:, lag : lag + samples]) / channels
    out_ref[...] = stacked
    power_ref[...] = jnp.sum(stacked * stacked, axis=1, keepdims=True)


def lag_kernels(templates):
    members, channels, window = templates.shape
    parts = window // LAG_BLOCK
    laid = templates.reshape(members, channels, parts, LAG_BLOCK)[..., ::-1]
    laid = jnp.transpose(laid, (1, 2, 0, 3)).astype(jnp.float32)
    centred = laid - jnp.mean(laid, axis=(1, 3), keepdims=True)
    norm = jnp.sqrt(jnp.sum(centred * centred, axis=(1, 3), keepdims=True) + 1e-06)
    return (centred / norm).astype(jnp.bfloat16).reshape(channels, parts * members, LAG_BLOCK)


def early_kernel(group_ref, tr_ref, out_ref, power_ref):
    pairs, channels, width = group_ref.shape

    def load_rows(first):
        return jnp.concatenate([group_ref[m, pl.ds(first, ROWS), :] for m in range(pairs)], axis=1)

    corr_kernel(load_rows, channels, pairs * width, tr_ref, out_ref, power_ref)


def late_kernel(group_ref, head_ref, tr_ref, out_ref, power_ref):
    pairs, channels, width = group_ref.shape
    samples = head_ref.shape[1]

    def load_rows(first):
        last = group_ref[pairs - 1, pl.ds(first, ROWS), :]
        return jnp.concatenate([last[:, width - samples :], head_ref[pl.ds(first, ROWS), :]], axis=1)

    corr_kernel(load_rows, channels, 2 * samples, tr_ref, out_ref, power_ref)


def stacked_correlation(group, head, kernels, window):
    pairs, channels, width = group.shape
    samples = head.shape[1]
    members = kernels.shape[1] * LAG_BLOCK // window
    sums = jax.ShapeDtypeStruct((members, 1), jnp.float32)
    early, early_power = pl.pallas_call(
        early_kernel,
        out_shape=(jax.ShapeDtypeStruct((members, pairs * width - samples), jnp.float32), sums),
    )(group, kernels)
    late, late_power = pl.pallas_call(
        late_kernel,
        out_shape=(jax.ShapeDtypeStruct((members, samples), jnp.float32), sums),
    )(group, head, kernels)
    return jnp.concatenate([early, late], axis=1), (early_power + late_power)[:, 0]


def seg_sum(value):
    nseg = lax.axis_size("seg")
    copies = jnp.broadcast_to(value[None], (nseg,) + value.shape)
    return jnp.sum(lax.all_to_all(copies, "seg", 0, 0, tiled=True), axis=0)


def body(record, templates):
    channels, samples = record.shape
    window = templates.shape[2]
    nblk = lax.axis_size(BLK)
    group, kernels = gather_group(record, lag_kernels(templates))
    head = next_group_head(group[0], samples)
    stacked, partial = stacked_correlation(group, head, kernels, window)
    power_sum = seg_sum(partial)
    record_len = samples * lax.axis_size("seg") * nblk
    detection = stacked / jnp.sqrt(power_sum / record_len + 1e-06)[:, None]
    members = detection.shape[0]
    pieces = detection.reshape(members, nblk, samples)
    spread = lax.all_to_all(pieces, BLK, 1, 0, tiled=True)
    return spread.reshape(members * nblk, samples)


BLK = ("bx", "bz")


def solution(mesh):
    nseg, nblk = mesh.shape["seg"], mesh.shape["blk"]
    split = Mesh(np.asarray(mesh.devices).reshape(nseg, nblk // 2, 2), ("seg",) + BLK)
    return jax.shard_map(
        body,
        mesh=split,
        in_specs=(P(None, ("seg",) + BLK), P(BLK, None, None)),
        out_specs=P(None, ("seg",) + BLK),
        check_vma=False,
    )
```
